512 devices in a mesh: row: 64 (over z_hi, y, x), col: 8 (over z_lo, core).
Axes of the slice: x: 4, y: 8, z: 8 (z_hi: 2, z_lo: 4; z = z_hi * 4 + z_lo), core: 2. Of those that a mesh axis runs over, the one named last changes fastest.
Arguments:
- queries: bfloat16 [64, 1024, 768], P('row', 'col'), may hold values from -20 to 20
- key_vectors: bfloat16 [64, 1024, 768], P('row', 'col'), may hold values from -20 to 20
- value_vectors: bfloat16 [64, 1024, 768], P('row', 'col'), may hold values from -6 to 6
- cotangent: bfloat16 [64, 1024, 768], P('row', 'col'), may hold values from -6 to 6
Outputs:
- attended: bfloat16 [64, 1024, 768], P('row', 'col')
- query_grad: bfloat16 [64, 1024, 768], P('row', 'col')
- key_grad: bfloat16 [64, 1024, 768], P('row', 'col')
- value_grad: bfloat16 [64, 1024, 768], P('row', 'col')
- logit_peak: float32 [12], replicated
The draws below stay inside these ranges and needn't reach their ends.
All inputs are finite; a program needn't handle non-finite values.
Results may differ from the reference program's by a relative error of at most 0.023.
Values may be sent and summed in bfloat16 or wider, within the bound.
No kernel may reach another device: no remote copies, remote signals or barrier semaphores. Data moves between devices by JAX's collectives and lax.ppermute only.
A program may use at most 128 MiB of HBM per device.

```python
import jax
import jax.numpy as jnp
from jax import lax

H = 12
HD = 64
DILATION_STEP = 16
HALF_EXTENT = 3
HH = 768
TOKEN_ROWS = 64
TOKEN_COLUMNS = 1024


def query_key_pair(key):
    base_key = jax.random.fold_in(key, 7)
    query_key, key_key, rough_key = jax.random.split(base_key, 3)
    shape = (TOKEN_ROWS, TOKEN_COLUMNS, H, HD)
    row_frac = jnp.arange(TOKEN_ROWS, dtype=jnp.float32)[:, None, None, None] / max(TOKEN_ROWS - 1, 1)
    lift = 1.0 + 0.8 * row_frac
    rough_query = jax.random.uniform(rough_key, (TOKEN_ROWS, TOKEN_COLUMNS, H, 1), jnp.float32, 0.6, 1.4)
    rough_keys = jax.random.uniform(jax.random.fold_in(rough_key, 1), (TOKEN_ROWS, TOKEN_COLUMNS, H, 1), jnp.float32, 0.6, 1.4)
    base_query = jax.random.truncated_normal(query_key, -4.0, 4.0, shape, jnp.float32)
    base_keys = jax.random.truncated_normal(key_key, -4.0, 4.0, shape, jnp.float32)
    query_out = base_query * lift * rough_query
    neighbour_keys = base_keys * lift * rough_keys
    return (query_out.reshape(TOKEN_ROWS, TOKEN_COLUMNS, H * HD), neighbour_keys.reshape(TOKEN_ROWS, TOKEN_COLUMNS, H * HD))


def draw_queries(key, part):
    return query_key_pair(key)[0].astype(jnp.bfloat16)


def draw_key_vectors(key, part):
    return query_key_pair(key)[1].astype(jnp.bfloat16)


def shard_levels(stream_key, shape, shards, low, top_value):
    factor_of = 1.0
    for dim, shards_of in shards:
        heights = jax.random.uniform(jax.random.fold_in(jax.random.fold_in(stream_key, 6), dim), (shards_of,), jnp.float32, low / len(shards), top_value / len(shards))
        factor_of = factor_of * jnp.repeat(jnp.exp(heights), shape[dim] // shards_of).reshape((-1,) + (1,) * (len(shape) - 1 - dim))
    return factor_of


def normal_values(rng, dims, spread, bound, pieces=(), kind=jnp.bfloat16):
    array = spread * jax.random.normal(rng, dims, jnp.float32)
    if pieces:
        array = array * shard_levels(rng, dims, pieces, -0.22, 0.18)
    return jnp.clip(array, -bound, bound).astype(kind)


def setup_inputs(seed: int = 0) -> dict:
    keys = jax.random.split(jax.random.key(seed), 5)
    queries = draw_queries(jax.random.fold_in(keys[4], 71), 0)
    key_vectors = draw_key_vectors(jax.random.fold_in(keys[4], 71), 0)
    value_vectors = normal_values(keys[2], (TOKEN_ROWS, TOKEN_COLUMNS, HH), 1.0, 6.0, ((0, 64), (1, 8)))
    cotangent = normal_values(keys[3], (TOKEN_ROWS, TOKEN_COLUMNS, HH), 1.0, 6.0, ((0, 64), (1, 8)))
    return {"queries": queries, "key_vectors": key_vectors, "value_vectors": value_vectors, "cotangent": cotangent}


def reference(queries, key_vectors, value_vectors, cotangent):
    neighbour_cells = HALF_EXTENT * DILATION_STEP
    logit_scale = HD ** -0.5
    head_shape = (TOKEN_ROWS, TOKEN_COLUMNS, H, HD)
    big_negative = -1.0e30
    query32 = queries.astype(jnp.float32).reshape(head_shape)
    cot32 = cotangent.astype(jnp.float32).reshape(head_shape)
    border = ((neighbour_cells, neighbour_cells), (neighbour_cells, neighbour_cells), (0, 0), (0, 0))
    key_pad = jnp.pad(key_vectors.astype(jnp.float32).reshape(head_shape), border)
    value_pad = jnp.pad(value_vectors.astype(jnp.float32).reshape(head_shape), border)
    row_indices = jnp.arange(TOKEN_ROWS, dtype=jnp.int32)
    column_indices = jnp.arange(TOKEN_COLUMNS, dtype=jnp.int32)
    offsets = [(row_shift, column_shift) for row_shift in range(-HALF_EXTENT, HALF_EXTENT + 1) for column_shift in range(-HALF_EXTENT, HALF_EXTENT + 1)]

    def near(padded, row_shift, column_shift):
        top_edge = neighbour_cells + row_shift * DILATION_STEP
        left_edge = neighbour_cells + column_shift * DILATION_STEP
        return padded[top_edge:top_edge + TOKEN_ROWS, left_edge:left_edge + TOKEN_COLUMNS]

    def usable(row_shift, column_shift):
        row_valid = (row_indices + row_shift * DILATION_STEP >= 0) & (row_indices + row_shift * DILATION_STEP < TOKEN_ROWS)
        column_valid = (column_indices + column_shift * DILATION_STEP >= 0) & (column_indices + column_shift * DILATION_STEP < TOKEN_COLUMNS)
        return (row_valid[:, None] & column_valid[None, :])[:, :, None]

    scores = []
    masks = []
    for row_shift, column_shift in offsets:
        scores.append(jnp.sum(query32 * near(key_pad, row_shift, column_shift), axis=-1) * logit_scale)
        masks.append(usable(row_shift, column_shift))
    row_max = jnp.full((TOKEN_ROWS, TOKEN_COLUMNS, H), big_negative, jnp.float32)
    logit_peak = jnp.full((H,), big_negative, jnp.float32)
    for score, mask in zip(scores, masks):
        masked = jnp.where(mask, score, big_negative)
        row_max = jnp.maximum(row_max, masked)
        logit_peak = jnp.maximum(logit_peak, jnp.max(masked, axis=(0, 1)))
    expos = [jnp.where(mask, jnp.exp(score - row_max), 0.0) for score, mask in zip(scores, masks)]
    total = jnp.zeros((TOKEN_ROWS, TOKEN_COLUMNS, H), jnp.float32)
    for expo in expos:
        total = total + expo
    weights = [expo / total for expo in expos]
    rounded = [lax.optimization_barrier(weight.astype(jnp.bfloat16)).astype(jnp.float32) for weight in weights]
    attended32 = jnp.zeros(head_shape, jnp.float32)
    for (row_shift, column_shift), weight_b in zip(offsets, rounded):
        attended32 = attended32 + weight_b[..., None] * near(value_pad, row_shift, column_shift)
    drive = jnp.sum(cot32 * attended32, axis=-1)
    query_grad = jnp.zeros(head_shape, jnp.float32)
    key_acc = jnp.zeros_like(key_pad)
    value_acc = jnp.zeros_like(value_pad)
    for (row_shift, column_shift), weight, weight_b in zip(offsets, weights, rounded):
        through = jnp.sum(cot32 * near(value_pad, row_shift, column_shift), axis=-1)
        slope = weight * (through - drive)
        slope_b = lax.optimization_barrier(slope.astype(jnp.bfloat16)).astype(jnp.float32)
        query_grad = query_grad + slope_b[..., None] * near(key_pad, row_shift, column_shift) * logit_scale
        top_edge = neighbour_cells + row_shift * DILATION_STEP
        left_edge = neighbour_cells + column_shift * DILATION_STEP
        key_acc = key_acc.at[top_edge:top_edge + TOKEN_ROWS, left_edge:left_edge + TOKEN_COLUMNS].add(slope_b[..., None] * query32 * logit_scale)
        value_acc = value_acc.at[top_edge:top_edge + TOKEN_ROWS, left_edge:left_edge + TOKEN_COLUMNS].add(weight_b[..., None] * cot32)
    key_grad = key_acc[neighbour_cells:neighbour_cells + TOKEN_ROWS, neighbour_cells:neighbour_cells + TOKEN_COLUMNS]
    value_grad = value_acc[neighbour_cells:neighbour_cells + TOKEN_ROWS, neighbour_cells:neighbour_cells + TOKEN_COLUMNS]
    flat = (TOKEN_ROWS, TOKEN_COLUMNS, H * HD)
    return (attended32.astype(jnp.bfloat16).reshape(flat),
            query_grad.astype(jnp.bfloat16).reshape(flat),
            key_grad.astype(jnp.bfloat16).reshape(flat),
            value_grad.astype(jnp.bfloat16).reshape(flat),
            logit_peak)
```

```python
import jax
import jax.numpy as jnp
from jax import lax
from jax.sharding import PartitionSpec as P

H = 12
HD = 64
DILATION_STEP = 16
HALF_EXTENT = 3


big_negative = -1e30


def passed_along(value, axis, steps):
    count = lax.axis_size(axis)
    first, last = (max(0, -steps), min(count, count - steps))
    return lax.ppermute(value, axis, [(source, source + steps) for source in range(first, last)])


def all_max(value, axes):
    for axis in axes:
        count = lax.axis_size(axis)
        if count & (count - 1):
            value = lax.pmax(value, axis)
            continue
        stride = 1
        while stride < count:
            partner = lax.ppermute(value, axis, [(i, i ^ stride) for i in range(count)])
            value = jnp.maximum(value, partner)
            stride *= 2
    return value


def extended(cells, sides, width):
    for axis, dim in sides:
        count = lax.axis_size(axis)
        ends = count - 1
        head = lax.slice_in_dim(cells, 0, width, axis=dim)
        tail = lax.slice_in_dim(cells, cells.shape[dim] - width, cells.shape[dim], axis=dim)
        cells = jnp.concatenate(
            [
                lax.ppermute(tail, axis, [(i, (i + 1) % count) for i in range(ends)]),
                cells,
                lax.ppermute(head, axis, [((i + 1) % count, i) for i in range(ends)]),
            ],
            axis=dim,
        )
    return cells


def spread_pairs(widened, step_length):
    blocks = {0: widened}
    for row_shift in range(-HALF_EXTENT, HALF_EXTENT + 1):
        if row_shift != 0:
            blocks[row_shift] = passed_along(widened, "row", -row_shift * step_length)
    return jnp.stack([blocks[row_shift] for row_shift in range(-HALF_EXTENT, HALF_EXTENT + 1)])


def return_rows(spill, step_length):
    limit = lax.axis_size("row")
    gathered = spill[HALF_EXTENT]
    for row_shift in range(-HALF_EXTENT, HALF_EXTENT + 1):
        if row_shift != 0 and abs(row_shift) * step_length < limit:
            gathered = gathered + passed_along(
                spill[row_shift + HALF_EXTENT].astype(jnp.bfloat16), "row", row_shift * step_length
            ).astype(jnp.float32)
    return gathered


def head_sums(product, indicator):
    return jnp.einsum("itf,fh->iht", product, indicator, precision=lax.Precision.HIGHEST)


def to_features(per_head):
    return jnp.repeat(jnp.swapaxes(per_head, -1, -2), HD, axis=-1)


def on_device(queries, key_vectors, value_vectors, cotangent):
    rows_per_shard, cols_dev, feature_count = queries.shape
    token_count = rows_per_shard * cols_dev
    neighbour_cells = HALF_EXTENT * DILATION_STEP
    step_length = DILATION_STEP // rows_per_shard
    window = 2 * HALF_EXTENT + 1
    logit_scale = HD ** (-0.5)
    row_total = rows_per_shard * lax.axis_size("row")
    col_total = cols_dev * lax.axis_size("col")
    row_place = lax.axis_index("row") * rows_per_shard + jnp.arange(rows_per_shard, dtype=jnp.int32)
    col_place = lax.axis_index("col") * cols_dev + jnp.arange(cols_dev, dtype=jnp.int32)
    shift_list = jnp.arange(-HALF_EXTENT, HALF_EXTENT + 1, dtype=jnp.int32) * DILATION_STEP
    row_target = row_place[None, :] + shift_list[:, None]
    col_target = col_place[None, :] + shift_list[:, None]
    row_usable = (row_target >= 0) & (row_target < row_total)
    col_usable = (col_target >= 0) & (col_target < col_total)
    usable = col_usable[:, None, None, :] & row_usable[None, :, :, None]
    indicator = (
        jnp.arange(feature_count, dtype=jnp.int32)[:, None] // HD
        == jnp.arange(H, dtype=jnp.int32)[None, :]
    ).astype(jnp.float32)
    pairs_in = jnp.concatenate([key_vectors, value_vectors], axis=-1)
    widened = extended(pairs_in, (("col", 1),), neighbour_cells)
    stacked = spread_pairs(widened, step_length)

    def column_block(column_stride):
        start_position = neighbour_cells + column_stride * DILATION_STEP
        piece = stacked[:, :, start_position : start_position + cols_dev].reshape(
            window, token_count, 2 * feature_count
        )
        return (
            piece[..., :feature_count].astype(jnp.float32),
            piece[..., feature_count:].astype(jnp.float32),
        )

    query32 = queries.reshape(token_count, feature_count).astype(jnp.float32)
    cot32 = cotangent.reshape(token_count, feature_count).astype(jnp.float32)
    score_list = []
    for column_stride in range(-HALF_EXTENT, HALF_EXTENT + 1):
        key_block, value_block = column_block(column_stride)
        score_list.append(head_sums(query32[None] * key_block, indicator) * logit_scale)
    scores = jnp.stack(score_list)
    masked = jnp.where(usable, scores, big_negative)
    row_max = jnp.max(masked, axis=(0, 1))
    local_peak = jnp.max(masked, axis=(0, 1, 3))
    logit_peak = all_max(local_peak, ("col", "row"))
    expo = jnp.where(usable, jnp.exp(scores - row_max), 0.0)
    total = jnp.sum(expo, axis=(0, 1))
    weights = expo / total
    weights_b = weights.astype(jnp.bfloat16)
    attended32 = jnp.zeros((token_count, feature_count), jnp.float32)
    for column_stride in range(-HALF_EXTENT, HALF_EXTENT + 1):
        key_block, value_block = column_block(column_stride)
        spread_w = to_features(weights_b[column_stride + HALF_EXTENT].astype(jnp.float32))
        attended32 = attended32 + jnp.sum(spread_w * value_block, axis=0)
    attended = attended32.astype(jnp.bfloat16).reshape(rows_per_shard, cols_dev, feature_count)
    drive = head_sums((cot32 * attended32)[None], indicator)[0]
    query_grad32 = jnp.zeros((token_count, feature_count), jnp.float32)
    slope_list = []
    for column_stride in range(-HALF_EXTENT, HALF_EXTENT + 1):
        key_block, value_block = column_block(column_stride)
        through = head_sums(cot32[None] * value_block, indicator)
        slope_b = (weights[column_stride + HALF_EXTENT] * (through - drive)).astype(jnp.bfloat16)
        slope_list.append(slope_b)
        query_grad32 = (
            query_grad32
            + jnp.sum(to_features(slope_b.astype(jnp.float32)) * key_block, axis=0) * logit_scale
        )
    query_grad = query_grad32.astype(jnp.bfloat16).reshape(rows_per_shard, cols_dev, feature_count)
    spill = jnp.zeros(
        (window, rows_per_shard, cols_dev + 2 * neighbour_cells, 2 * feature_count), jnp.float32
    )
    for column_stride in range(-HALF_EXTENT, HALF_EXTENT + 1):
        slot = column_stride + HALF_EXTENT
        start_position = neighbour_cells + column_stride * DILATION_STEP
        key_part = to_features(slope_list[slot].astype(jnp.float32)) * query32[None] * logit_scale
        value_part = to_features(weights_b[slot].astype(jnp.float32)) * cot32[None]
        both = jnp.concatenate([key_part, value_part], axis=-1).reshape(
            window, rows_per_shard, cols_dev, 2 * feature_count
        )
        spill = spill + jnp.pad(
            both, ((0, 0), (0, 0), (start_position, 2 * neighbour_cells - start_position), (0, 0))
        )
    gathered = return_rows(spill, step_length)
    west_part = gathered[:, :neighbour_cells]
    east_part = gathered[:, neighbour_cells + cols_dev :]
    owned = gathered[:, neighbour_cells : neighbour_cells + cols_dev]
    from_east = passed_along(west_part.astype(jnp.bfloat16), "col", -1).astype(west_part.dtype)
    from_west = passed_along(east_part.astype(jnp.bfloat16), "col", 1).astype(east_part.dtype)
    owned = owned.at[:, cols_dev - neighbour_cells :].add(from_east)
    owned = owned.at[:, :neighbour_cells].add(from_west)
    key_grad = owned[..., :feature_count].astype(jnp.bfloat16)
    value_grad = owned[..., feature_count:].astype(jnp.bfloat16)
    return (attended, query_grad, key_grad, value_grad, logit_peak)


def solution(mesh):
    placed = (
        P("row", "col", None),
        P("row", "col", None),
        P("row", "col", None),
        P("row", "col", None),
    )
    return jax.shard_map(
        on_device,
        mesh=mesh,
        in_specs=placed,
        out_specs=(
            P("row", "col", None),
            P("row", "col", None),
            P("row", "col", None),
            P("row", "col", None),
            P(),
        ),
        check_vma=False,
    )
```

```python
import jax
import jax.numpy as jnp
from jax import lax
from jax.sharding import PartitionSpec as P
from jax.experimental import pallas as pl
from jax.experimental.pallas import tpu as pltpu

H = 12
HD = 64
DILATION_STEP = 16
HALF_EXTENT = 3


big_negative = -1e30


def passed_along(value, axis, steps):
    count = lax.axis_size(axis)
    first, last = (max(0, -steps), min(count, count - steps))
    return lax.ppermute(value, axis, [(source, source + steps) for source in range(first, last)])


def all_max(value, axes):
    for axis in axes:
        count = lax.axis_size(axis)
        if count & (count - 1):
            value = lax.pmax(value, axis)
            continue
        stride = 1
        while stride < count:
            partner = lax.ppermute(value, axis, [(i, i ^ stride) for i in range(count)])
            value = jnp.maximum(value, partner)
            stride *= 2
    return value


def extended(cells, sides, width):
    for axis, dim in sides:
        count = lax.axis_size(axis)
        ends = count - 1
        head = lax.slice_in_dim(cells, 0, width, axis=dim)
        tail = lax.slice_in_dim(cells, cells.shape[dim] - width, cells.shape[dim], axis=dim)
        cells = jnp.concatenate(
            [
                lax.ppermute(tail, axis, [(i, (i + 1) % count) for i in range(ends)]),
                cells,
                lax.ppermute(head, axis, [((i + 1) % count, i) for i in range(ends)]),
            ],
            axis=dim,
        )
    return cells


def spread_pairs(widened, step_length):
    blocks = {0: widened}
    for row_shift in range(-HALF_EXTENT, HALF_EXTENT + 1):
        if row_shift != 0:
            blocks[row_shift] = passed_along(widened, "row", -row_shift * step_length)
    return jnp.stack([blocks[row_shift] for row_shift in range(-HALF_EXTENT, HALF_EXTENT + 1)])


def return_rows(spill, step_length):
    limit = lax.axis_size("row")
    gathered = spill[HALF_EXTENT]
    for row_shift in range(-HALF_EXTENT, HALF_EXTENT + 1):
        if row_shift != 0 and abs(row_shift) * step_length < limit:
            gathered = gathered + passed_along(
                spill[row_shift + HALF_EXTENT].astype(jnp.bfloat16), "row", row_shift * step_length
            ).astype(jnp.float32)
    return gathered


def head_sums(product, indicator):
    return jnp.einsum("itf,fh->iht", product, indicator, precision=lax.Precision.HIGHEST)


def to_features(per_head):
    return jnp.repeat(jnp.swapaxes(per_head, -1, -2), HD, axis=-1)


LANES = 128


def neighbourhood_body(q_ref, c_ref, kv_ref, mask_ref, att_ref, qg_ref, spill_ref, peak_ref, s_scr):
    f32, bf16 = jnp.float32, jnp.bfloat16
    token_count, feature_count = q_ref.shape
    window = 2 * HALF_EXTENT + 1
    logit_scale = HD ** (-0.5)
    ind = (
        lax.broadcasted_iota(jnp.int32, (feature_count, LANES), 0) // HD
        == lax.broadcasted_iota(jnp.int32, (feature_count, LANES), 1)
    ).astype(bf16)
    ind_t = (
        lax.broadcasted_iota(jnp.int32, (LANES, feature_count), 1) // HD
        == lax.broadcasted_iota(jnp.int32, (LANES, feature_count), 0)
    ).astype(bf16)

    def mm(x, y):
        return jnp.dot(x, y, preferred_element_type=f32)

    def exact_sum(p):
        hi = p.astype(bf16)
        lo = (p - hi.astype(f32)).astype(bf16)
        return mm(hi, ind) + mm(lo, ind)

    def full_sum(p):
        hi = p.astype(bf16)
        r1 = p - hi.astype(f32)
        mid = r1.astype(bf16)
        lo = (r1 - mid.astype(f32)).astype(bf16)
        return mm(hi, ind) + mm(mid, ind) + mm(lo, ind)

    def spread(w):
        return mm(w, ind_t)

    def keys(a, b):
        return kv_ref[a, pl.ds(b * DILATION_STEP, token_count), pl.ds(0, feature_count)].astype(f32)

    def values(a, b):
        return kv_ref[a, pl.ds(b * DILATION_STEP, token_count), pl.ds(feature_count, feature_count)].astype(f32)

    q = q_ref[...].astype(f32)
    c = c_ref[...].astype(f32)
    top = jnp.full((token_count, LANES), big_negative, f32)
    for a in range(window):
        for b in range(window):
            s = exact_sum(q * keys(a, b)) * logit_scale
            s = jnp.where(mask_ref[a * window + b] > 0, s, big_negative)
            s_scr[a * window + b] = s
            top = jnp.maximum(top, s)
    peak_ref[...] = jnp.max(top, axis=0, keepdims=True)
    total = jnp.zeros((token_count, LANES), f32)
    for ab in range(window * window):
        e = jnp.where(mask_ref[ab] > 0, jnp.exp(s_scr[ab] - top), 0.0)
        s_scr[ab] = e
        total = total + e
    att = jnp.zeros((token_count, feature_count), f32)
    for a in range(window):
        for b in range(window):
            w_b = (s_scr[a * window + b] / total).astype(bf16)
            att = att + spread(w_b) * values(a, b)
    att_ref[...] = att.astype(att_ref.dtype)
    drive = full_sum(c * att)
    spill_ref[...] = jnp.zeros(spill_ref.shape, f32)
    qg = jnp.zeros((token_count, feature_count), f32)
    for a in range(window):
        for b in range(window):
            w = s_scr[a * window + b] / total
            v = values(a, b)
            through = exact_sum(c * v)
            slope = spread((w * (through - drive)).astype(bf16))
            qg = qg + slope * keys(a, b)
            rows = pl.ds(b * DILATION_STEP, token_count)
            spill_ref[a, rows, pl.ds(0, feature_count)] += slope * q * logit_scale
            spill_ref[a, rows, pl.ds(feature_count, feature_count)] += spread(w.astype(bf16)) * c
    qg_ref[...] = (qg * logit_scale).astype(qg_ref.dtype)


def neighbourhood_kernel(q, c, kv, mask, interpret=False):
    token_count, feature_count = q.shape
    window = kv.shape[0]
    vmem = pltpu.MemorySpace.VMEM if hasattr(pltpu, "MemorySpace") else pltpu.TPUMemorySpace.VMEM
    spec = pl.BlockSpec(memory_space=vmem)
    return pl.pallas_call(
        neighbourhood_body,
        out_shape=(
            jax.ShapeDtypeStruct((token_count, feature_count), jnp.bfloat16),
            jax.ShapeDtypeStruct((token_count, feature_count), jnp.bfloat16),
            jax.ShapeDtypeStruct(kv.shape, jnp.float32),
            jax.ShapeDtypeStruct((1, LANES), jnp.float32),
        ),
        in_specs=[spec] * 4,
        out_specs=(spec,) * 4,
        scratch_shapes=[pltpu.VMEM((window * window, token_count, LANES), jnp.float32)],
        compiler_params=pltpu.CompilerParams(vmem_limit_bytes=56 * 1024 * 1024),
        interpret=interpret,
    )(q, c, kv, mask)


def on_device(queries, key_vectors, value_vectors, cotangent):
    rows_per_shard, cols_dev, feature_count = queries.shape
    token_count = rows_per_shard * cols_dev
    neighbour_cells = HALF_EXTENT * DILATION_STEP
    step_length = DILATION_STEP // rows_per_shard
    window = 2 * HALF_EXTENT + 1
    logit_scale = HD ** (-0.5)
    row_total = rows_per_shard * lax.axis_size("row")
    col_total = cols_dev * lax.axis_size("col")
    row_place = lax.axis_index("row") * rows_per_shard + jnp.arange(rows_per_shard, dtype=jnp.int32)
    col_place = lax.axis_index("col") * cols_dev + jnp.arange(cols_dev, dtype=jnp.int32)
    shift_list = jnp.arange(-HALF_EXTENT, HALF_EXTENT + 1, dtype=jnp.int32) * DILATION_STEP
    row_target = row_place[None, :] + shift_list[:, None]
    col_target = col_place[None, :] + shift_list[:, None]
    row_usable = (row_target >= 0) & (row_target < row_total)
    col_usable = (col_target >= 0) & (col_target < col_total)
    usable = col_usable[:, None, None, :] & row_usable[None, :, :, None]
    pairs_in = jnp.concatenate([key_vectors, value_vectors], axis=-1)
    widened = extended(pairs_in, (("col", 1),), neighbour_cells)
    stacked = spread_pairs(widened, step_length)

    tokens = lax.broadcasted_iota(jnp.int32, (window * window, token_count, LANES), 2) < H
    usable_ab = jnp.transpose(usable[:, :, 0, :], (1, 0, 2)).reshape(window * window, token_count)
    mask = jnp.where(tokens, usable_ab[..., None], True).astype(jnp.float32)
    attended, query_grad, spill, peak = neighbourhood_kernel(
        queries.reshape(token_count, feature_count),
        cotangent.reshape(token_count, feature_count),
        stacked.reshape(window, cols_dev + 2 * neighbour_cells, 2 * feature_count),
        mask,
    )
    attended = attended.reshape(rows_per_shard, cols_dev, feature_count)
    query_grad = query_grad.reshape(rows_per_shard, cols_dev, feature_count)
    logit_peak = all_max(peak[0, :H], ("col", "row"))
    spill = spill.reshape(window, rows_per_shard, cols_dev + 2 * neighbour_cells, 2 * feature_count)
    gathered = return_rows(spill, step_length)
    west_part = gathered[:, :neighbour_cells]
    east_part = gathered[:, neighbour_cells + cols_dev :]
    owned = gathered[:, neighbour_cells : neighbour_cells + cols_dev]
    from_east = passed_along(west_part.astype(jnp.bfloat16), "col", -1).astype(west_part.dtype)
    from_west = passed_along(east_part.astype(jnp.bfloat16), "col", 1).astype(east_part.dtype)
    owned = owned.at[:, cols_dev - neighbour_cells :].add(from_east)
    owned = owned.at[:, :neighbour_cells].add(from_west)
    key_grad = owned[..., :feature_count].astype(jnp.bfloat16)
    value_grad = owned[..., feature_count:].astype(jnp.bfloat16)
    return (attended, query_grad, key_grad, value_grad, logit_peak)


def solution(mesh):
    placed = (
        P("row", "col", None),
        P("row", "col", None),
        P("row", "col", None),
        P("row", "col", None),
    )
    return jax.shard_map(
        on_device,
        mesh=mesh,
        in_specs=placed,
        out_specs=(
            P("row", "col", None),
            P("row", "col", None),
            P("row", "col", None),
            P("row", "col", None),
            P(),
        ),
        check_vma=False,
    )
```

```python
import jax
import jax.numpy as jnp
from jax import lax
from jax.sharding import PartitionSpec as P
from jax.experimental import pallas as pl
from jax.experimental.pallas import tpu as pltpu

H = 12
HD = 64
DILATION_STEP = 16
HALF_EXTENT = 3


big_negative = -1e30


def passed_along(value, axis, steps):
    count = lax.axis_size(axis)
    first, last = (max(0, -steps), min(count, count - steps))
    return lax.ppermute(value, axis, [(source, source + steps) for source in range(first, last)])


def all_max(value, axes):
    for axis in axes:
        count = lax.axis_size(axis)
        if count & (count - 1):
            value = lax.pmax(value, axis)
            continue
        stride = 1
        while stride < count:
            radix = min(8, count // stride)
            group = stride * radix
            parts = [value]
            for step in range(1, radix):
                pairs = [
                    (i, (i // group) * group + ((i // stride + step) % radix) * stride + i % stride)
                    for i in range(count)
                ]
                parts.append(lax.ppermute(value, axis, pairs))
            for part in parts[1:]:
                value = jnp.maximum(value, part)
            stride = group
    return value


def extended(cells, sides, width):
    for axis, dim in sides:
        count = lax.axis_size(axis)
        ends = count - 1
        head = lax.slice_in_dim(cells, 0, width, axis=dim)
        tail = lax.slice_in_dim(cells, cells.shape[dim] - width, cells.shape[dim], axis=dim)
        cells = jnp.concatenate(
            [
                lax.ppermute(tail, axis, [(i, (i + 1) % count) for i in range(ends)]),
                cells,
                lax.ppermute(head, axis, [((i + 1) % count, i) for i in range(ends)]),
            ],
            axis=dim,
        )
    return cells


def spread_pairs(widened, step_length):
    blocks = {0: widened}
    for row_shift in range(-HALF_EXTENT, HALF_EXTENT + 1):
        if row_shift != 0:
            blocks[row_shift] = passed_along(widened, "row", -row_shift * step_length)
    return jnp.stack([blocks[row_shift] for row_shift in range(-HALF_EXTENT, HALF_EXTENT + 1)])


def return_rows(spill, step_length):
    limit = lax.axis_size("row")
    gathered = spill[HALF_EXTENT]
    for row_shift in range(-HALF_EXTENT, HALF_EXTENT + 1):
        if row_shift != 0 and abs(row_shift) * step_length < limit:
            gathered = gathered + passed_along(
                spill[row_shift + HALF_EXTENT].astype(jnp.bfloat16), "row", row_shift * step_length
            ).astype(jnp.float32)
    return gathered


def head_sums(product, indicator):
    return jnp.einsum("itf,fh->iht", product, indicator, precision=lax.Precision.HIGHEST)


def to_features(per_head):
    return jnp.repeat(jnp.swapaxes(per_head, -1, -2), HD, axis=-1)


LANES = 128


def neighbourhood_body(q_ref, c_ref, kv_ref, mask_ref, att_ref, qg_ref, spill_ref, peak_ref, s_scr):
    f32, bf16 = jnp.float32, jnp.bfloat16
    token_count, feature_count = q_ref.shape
    window = 2 * HALF_EXTENT + 1
    logit_scale = HD ** (-0.5)
    ind = (
        lax.broadcasted_iota(jnp.int32, (feature_count, LANES), 0) // HD
        == lax.broadcasted_iota(jnp.int32, (feature_count, LANES), 1)
    ).astype(bf16)
    ind_t = (
        lax.broadcasted_iota(jnp.int32, (LANES, feature_count), 1) // HD
        == lax.broadcasted_iota(jnp.int32, (LANES, feature_count), 0)
    ).astype(bf16)

    def mm(x, y):
        return jnp.dot(x, y, preferred_element_type=f32)

    def exact_sum(p):
        hi = p.astype(bf16)
        lo = (p - hi.astype(f32)).astype(bf16)
        return mm(hi, ind) + mm(lo, ind)

    def full_sum(p):
        hi = p.astype(bf16)
        r1 = p - hi.astype(f32)
        mid = r1.astype(bf16)
        lo = (r1 - mid.astype(f32)).astype(bf16)
        return mm(hi, ind) + mm(mid, ind) + mm(lo, ind)

    def spread(w):
        return mm(w, ind_t)

    def keys(a, b):
        return kv_ref[a, pl.ds(b * DILATION_STEP, token_count), pl.ds(0, feature_count)].astype(f32)

    def values(a, b):
        return kv_ref[a, pl.ds(b * DILATION_STEP, token_count), pl.ds(feature_count, feature_count)].astype(f32)

    q = q_ref[...].astype(f32)
    c = c_ref[...].astype(f32)
    top = jnp.full((token_count, LANES), big_negative, f32)
    for a in range(window):
        for b in range(window):
            s = exact_sum(q * keys(a, b)) * logit_scale
            s = jnp.where(mask_ref[a * window + b] > 0, s, big_negative)
            s_scr[a * window + b] = s
            top = jnp.maximum(top, s)
    peak_ref[...] = jnp.max(top, axis=0, keepdims=True)
    total = jnp.zeros((token_count, LANES), f32)
    for ab in range(window * window):
        e = jnp.where(mask_ref[ab] > 0, jnp.exp(s_scr[ab] - top), 0.0)
        s_scr[ab] = e
        total = total + e
    att = jnp.zeros((token_count, feature_count), f32)
    for a in range(window):
        for b in range(window):
            w_b = (s_scr[a * window + b] / total).astype(bf16)
            att = att + spread(w_b) * values(a, b)
    att_ref[...] = att.astype(att_ref.dtype)
    drive = full_sum(c * att)
    spill_ref[...] = jnp.zeros(spill_ref.shape, f32)
    qg = jnp.zeros((token_count, feature_count), f32)
    for a in range(window):
        for b in range(window):
            w = s_scr[a * window + b] / total
            v = values(a, b)
            through = exact_sum(c * v)
            slope = spread((w * (through - drive)).astype(bf16))
            qg = qg + slope * keys(a, b)
            rows = pl.ds(b * DILATION_STEP, token_count)
            spill_ref[a, rows, pl.ds(0, feature_count)] += slope * q * logit_scale
            spill_ref[a, rows, pl.ds(feature_count, feature_count)] += spread(w.astype(bf16)) * c
    qg_ref[...] = (qg * logit_scale).astype(qg_ref.dtype)


def neighbourhood_kernel(q, c, kv, mask, interpret=False):
    token_count, feature_count = q.shape
    window = kv.shape[0]
    vmem = pltpu.MemorySpace.VMEM if hasattr(pltpu, "MemorySpace") else pltpu.TPUMemorySpace.VMEM
    spec = pl.BlockSpec(memory_space=vmem)
    return pl.pallas_call(
        neighbourhood_body,
        out_shape=(
            jax.ShapeDtypeStruct((token_count, feature_count), jnp.bfloat16),
            jax.ShapeDtypeStruct((token_count, feature_count), jnp.bfloat16),
            jax.ShapeDtypeStruct(kv.shape, jnp.float32),
            jax.ShapeDtypeStruct((1, LANES), jnp.float32),
        ),
        in_specs=[spec] * 4,
        out_specs=(spec,) * 4,
        scratch_shapes=[pltpu.VMEM((window * window, token_count, LANES), jnp.float32)],
        compiler_params=pltpu.CompilerParams(vmem_limit_bytes=56 * 1024 * 1024),
        interpret=interpret,
    )(q, c, kv, mask)


def on_device(queries, key_vectors, value_vectors, cotangent):
    rows_per_shard, cols_dev, feature_count = queries.shape
    token_count = rows_per_shard * cols_dev
    neighbour_cells = HALF_EXTENT * DILATION_STEP
    step_length = DILATION_STEP // rows_per_shard
    window = 2 * HALF_EXTENT + 1
    logit_scale = HD ** (-0.5)
    row_total = rows_per_shard * lax.axis_size("row")
    col_total = cols_dev * lax.axis_size("col")
    row_place = lax.axis_index("row") * rows_per_shard + jnp.arange(rows_per_shard, dtype=jnp.int32)
    col_place = lax.axis_index("col") * cols_dev + jnp.arange(cols_dev, dtype=jnp.int32)
    shift_list = jnp.arange(-HALF_EXTENT, HALF_EXTENT + 1, dtype=jnp.int32) * DILATION_STEP
    row_target = row_place[None, :] + shift_list[:, None]
    col_target = col_place[None, :] + shift_list[:, None]
    row_usable = (row_target >= 0) & (row_target < row_total)
    col_usable = (col_target >= 0) & (col_target < col_total)
    usable = col_usable[:, None, None, :] & row_usable[None, :, :, None]
    pairs_in = jnp.concatenate([key_vectors, value_vectors], axis=-1)
    stacked = extended(spread_pairs(pairs_in, step_length), (("col", 2),), neighbour_cells)

    tokens = lax.broadcasted_iota(jnp.int32, (window * window, token_count, LANES), 2) < H
    usable_ab = jnp.transpose(usable[:, :, 0, :], (1, 0, 2)).reshape(window * window, token_count)
    mask = jnp.where(tokens, usable_ab[..., None], True).astype(jnp.float32)
    attended, query_grad, spill, peak = neighbourhood_kernel(
        queries.reshape(token_count, feature_count),
        cotangent.reshape(token_count, feature_count),
        stacked.reshape(window, cols_dev + 2 * neighbour_cells, 2 * feature_count),
        mask,
    )
    attended = attended.reshape(rows_per_shard, cols_dev, feature_count)
    query_grad = query_grad.reshape(rows_per_shard, cols_dev, feature_count)
    logit_peak = all_max(peak[0, :H], ("col", "row"))
    spill = spill.reshape(window, rows_per_shard, cols_dev + 2 * neighbour_cells, 2 * feature_count)
    west_part = spill[:, :, :neighbour_cells]
    east_part = spill[:, :, neighbour_cells + cols_dev :]
    owned = spill[:, :, neighbour_cells : neighbour_cells + cols_dev]
    from_east = passed_along(west_part.astype(jnp.bfloat16), "col", -1).astype(west_part.dtype)
    from_west = passed_along(east_part.astype(jnp.bfloat16), "col", 1).astype(east_part.dtype)
    owned = owned.at[:, :, cols_dev - neighbour_cells :].add(from_east)
    owned = owned.at[:, :, :neighbour_cells].add(from_west)
    owned = return_rows(owned, step_length)
    key_grad = owned[..., :feature_count].astype(jnp.bfloat16)
    value_grad = owned[..., feature_count:].astype(jnp.bfloat16)
    return (attended, query_grad, key_grad, value_grad, logit_peak)


def solution(mesh):
    placed = (
        P("row", "col", None),
        P("row", "col", None),
        P("row", "col", None),
        P("row", "col", None),
    )
    return jax.shard_map(
        on_device,
        mesh=mesh,
        in_specs=placed,
        out_specs=(
            P("row", "col", None),
            P("row", "col", None),
            P("row", "col", None),
            P("row", "col", None),
            P(),
        ),
        check_vma=False,
    )
```

```python
import jax
import jax.numpy as jnp
from jax import lax
from jax.sharding import PartitionSpec as P
from jax.experimental import pallas as pl
from jax.experimental.pallas import tpu as pltpu

H = 12
HD = 64
DILATION_STEP = 16
HALF_EXTENT = 3


big_negative = -1e30


def passed_along(value, axis, steps):
    count = lax.axis_size(axis)
    first, last = (max(0, -steps), min(count, count - steps))
    return lax.ppermute(value, axis, [(source, source + steps) for source in range(first, last)])


def all_max(value, axes):
    for axis in axes:
        count = lax.axis_size(axis)
        if count & (count - 1):
            value = lax.pmax(value, axis)
            continue
        stride = 1
        while stride < count:
            partner = lax.ppermute(value, axis, [(i, i ^ stride) for i in range(count)])
            value = jnp.maximum(value, partner)
            stride *= 2
    return value


def extended(cells, sides, width):
    for axis, dim in sides:
        count = lax.axis_size(axis)
        ends = count - 1
        head = lax.slice_in_dim(cells, 0, width, axis=dim)
        tail = lax.slice_in_dim(cells, cells.shape[dim] - width, cells.shape[dim], axis=dim)
        cells = jnp.concatenate(
            [
                lax.ppermute(tail, axis, [(i, (i + 1) % count) for i in range(ends)]),
                cells,
                lax.ppermute(head, axis, [((i + 1) % count, i) for i in range(ends)]),
            ],
            axis=dim,
        )
    return cells


def spread_pairs(widened, step_length):
    blocks = {0: widened}
    for row_shift in range(-HALF_EXTENT, HALF_EXTENT + 1):
        if row_shift != 0:
            blocks[row_shift] = passed_along(widened, "row", -row_shift * step_length)
    return jnp.stack([blocks[row_shift] for row_shift in range(-HALF_EXTENT, HALF_EXTENT + 1)])


def return_rows(spill, step_length):
    limit = lax.axis_size("row")
    gathered = spill[HALF_EXTENT]
    for row_shift in range(-HALF_EXTENT, HALF_EXTENT + 1):
        if row_shift != 0 and abs(row_shift) * step_length < limit:
            gathered = gathered + passed_along(
                spill[row_shift + HALF_EXTENT].astype(jnp.bfloat16), "row", row_shift * step_length
            ).astype(jnp.float32)
    return gathered


def head_sums(product, indicator):
    return jnp.einsum("itf,fh->iht", product, indicator, precision=lax.Precision.HIGHEST)


def to_features(per_head):
    return jnp.repeat(jnp.swapaxes(per_head, -1, -2), HD, axis=-1)


LANES = 128


def neighbourhood_body(q_ref, c_ref, kv_ref, mask_ref, att_ref, qg_ref, spill_ref, peak_ref, s_scr):
    f32, bf16 = jnp.float32, jnp.bfloat16
    token_count, feature_count = q_ref.shape
    window = 2 * HALF_EXTENT + 1
    logit_scale = HD ** (-0.5)
    ind = (
        lax.broadcasted_iota(jnp.int32, (feature_count, LANES), 0) // HD
        == lax.broadcasted_iota(jnp.int32, (feature_count, LANES), 1)
    ).astype(bf16)
    ind_t = (
        lax.broadcasted_iota(jnp.int32, (LANES, feature_count), 1) // HD
        == lax.broadcasted_iota(jnp.int32, (LANES, feature_count), 0)
    ).astype(bf16)

    def mm(x, y):
        return jnp.dot(x, y, preferred_element_type=f32)

    def exact_sum(p):
        hi = p.astype(bf16)
        lo = (p - hi.astype(f32)).astype(bf16)
        return mm(hi, ind) + mm(lo, ind)

    def full_sum(p):
        hi = p.astype(bf16)
        r1 = p - hi.astype(f32)
        mid = r1.astype(bf16)
        lo = (r1 - mid.astype(f32)).astype(bf16)
        return mm(hi, ind) + mm(mid, ind) + mm(lo, ind)

    def spread(w):
        return mm(w, ind_t)

    def keys(a, b):
        return kv_ref[a, pl.ds(b * DILATION_STEP, token_count), pl.ds(0, feature_count)].astype(f32)

    def values(a, b):
        return kv_ref[a, pl.ds(b * DILATION_STEP, token_count), pl.ds(feature_count, feature_count)].astype(f32)

    q = q_ref[...].astype(f32)
    c = c_ref[...].astype(f32)
    top = jnp.full((token_count, LANES), big_negative, f32)
    for a in range(window):
        for b in range(window):
            s = exact_sum(q * keys(a, b)) * logit_scale
            s = jnp.where(mask_ref[a * window + b] > 0, s, big_negative)
            s_scr[a * window + b] = s
            top = jnp.maximum(top, s)
    peak_ref[...] = jnp.max(top, axis=0, keepdims=True)
    total = jnp.zeros((token_count, LANES), f32)
    for ab in range(window * window):
        e = jnp.where(mask_ref[ab] > 0, jnp.exp(s_scr[ab] - top), 0.0)
        s_scr[ab] = e
        total = total + e
    att = jnp.zeros((token_count, feature_count), f32)
    for a in range(window):
        for b in range(window):
            w_b = (s_scr[a * window + b] / total).astype(bf16)
            att = att + spread(w_b) * values(a, b)
    att_ref[...] = att.astype(att_ref.dtype)
    drive = full_sum(c * att)
    spill_ref[...] = jnp.zeros(spill_ref.shape, f32)
    qg = jnp.zeros((token_count, feature_count), f32)
    for a in range(window):
        for b in range(window):
            w = s_scr[a * window + b] / total
            v = values(a, b)
            through = exact_sum(c * v)
            slope = spread((w * (through - drive)).astype(bf16))
            qg = qg + slope * keys(a, b)
            rows = pl.ds(b * DILATION_STEP, token_count)
            spill_ref[a, rows, pl.ds(0, feature_count)] += slope * q * logit_scale
            spill_ref[a, rows, pl.ds(feature_count, feature_count)] += spread(w.astype(bf16)) * c
    qg_ref[...] = (qg * logit_scale).astype(qg_ref.dtype)


def neighbourhood_kernel(q, c, kv, mask, interpret=False):
    token_count, feature_count = q.shape
    window = kv.shape[0]
    vmem = pltpu.MemorySpace.VMEM if hasattr(pltpu, "MemorySpace") else pltpu.TPUMemorySpace.VMEM
    spec = pl.BlockSpec(memory_space=vmem)
    return pl.pallas_call(
        neighbourhood_body,
        out_shape=(
            jax.ShapeDtypeStruct((token_count, feature_count), jnp.bfloat16),
            jax.ShapeDtypeStruct((token_count, feature_count), jnp.bfloat16),
            jax.ShapeDtypeStruct(kv.shape, jnp.float32),
            jax.ShapeDtypeStruct((1, LANES), jnp.float32),
        ),
        in_specs=[spec] * 4,
        out_specs=(spec,) * 4,
        scratch_shapes=[pltpu.VMEM((window * window, token_count, LANES), jnp.float32)],
        compiler_params=pltpu.CompilerParams(vmem_limit_bytes=56 * 1024 * 1024),
        interpret=interpret,
    )(q, c, kv, mask)


def on_device(queries, key_vectors, value_vectors, cotangent):
    rows_per_shard, cols_dev, feature_count = queries.shape
    token_count = rows_per_shard * cols_dev
    neighbour_cells = HALF_EXTENT * DILATION_STEP
    step_length = DILATION_STEP // rows_per_shard
    window = 2 * HALF_EXTENT + 1
    logit_scale = HD ** (-0.5)
    row_total = rows_per_shard * lax.axis_size("row")
    col_total = cols_dev * lax.axis_size("col")
    row_place = lax.axis_index("row") * rows_per_shard + jnp.arange(rows_per_shard, dtype=jnp.int32)
    col_place = lax.axis_index("col") * cols_dev + jnp.arange(cols_dev, dtype=jnp.int32)
    shift_list = jnp.arange(-HALF_EXTENT, HALF_EXTENT + 1, dtype=jnp.int32) * DILATION_STEP
    row_target = row_place[None, :] + shift_list[:, None]
    col_target = col_place[None, :] + shift_list[:, None]
    row_usable = (row_target >= 0) & (row_target < row_total)
    col_usable = (col_target >= 0) & (col_target < col_total)
    usable = col_usable[:, None, None, :] & row_usable[None, :, :, None]
    pairs_in = jnp.concatenate([key_vectors, value_vectors], axis=-1)
    stacked = extended(spread_pairs(pairs_in, step_length), (("col", 2),), neighbour_cells)

    tokens = lax.broadcasted_iota(jnp.int32, (window * window, token_count, LANES), 2) < H
    usable_ab = jnp.transpose(usable[:, :, 0, :], (1, 0, 2)).reshape(window * window, token_count)
    mask = jnp.where(tokens, usable_ab[..., None], True).astype(jnp.float32)
    attended, query_grad, spill, peak = neighbourhood_kernel(
        queries.reshape(token_count, feature_count),
        cotangent.reshape(token_count, feature_count),
        stacked.reshape(window, cols_dev + 2 * neighbour_cells, 2 * feature_count),
        mask,
    )
    attended = attended.reshape(rows_per_shard, cols_dev, feature_count)
    query_grad = query_grad.reshape(rows_per_shard, cols_dev, feature_count)
    spill = spill.reshape(window, rows_per_shard, cols_dev + 2 * neighbour_cells, 2 * feature_count)
    west_part = spill[:, :, :neighbour_cells]
    east_part = spill[:, :, neighbour_cells + cols_dev :]
    owned = spill[:, :, neighbour_cells : neighbour_cells + cols_dev]
    from_east = passed_along(west_part.astype(jnp.bfloat16), "col", -1).astype(west_part.dtype)
    from_west = passed_along(east_part.astype(jnp.bfloat16), "col", 1).astype(east_part.dtype)
    peak, from_east, from_west = lax.optimization_barrier((peak, from_east, from_west))
    owned = owned.at[:, :, cols_dev - neighbour_cells :].add(from_east)
    owned = owned.at[:, :, :neighbour_cells].add(from_west)
    owned = return_rows(owned, step_length)
    logit_peak = all_max(peak[0, :H], ("col", "row"))
    key_grad = owned[..., :feature_count].astype(jnp.bfloat16)
    value_grad = owned[..., feature_count:].astype(jnp.bfloat16)
    return (attended, query_grad, key_grad, value_grad, logit_peak)


def solution(mesh):
    placed = (
        P("row", "col", None),
        P("row", "col", None),
        P("row", "col", None),
        P("row", "col", None),
    )
    return jax.shard_map(
        on_device,
        mesh=mesh,
        in_specs=placed,
        out_specs=(
            P("row", "col", None),
            P("row", "col", None),
            P("row", "col", None),
            P("row", "col", None),
            P(),
        ),
        check_vma=False,
    )
```

```python
import jax
import jax.numpy as jnp
from jax import lax
from jax.sharding import PartitionSpec as P
from jax.experimental import pallas as pl
from jax.experimental.pallas import tpu as pltpu

H = 12
HD = 64
DILATION_STEP = 16
HALF_EXTENT = 3


big_negative = -1e30


def passed_along(value, axis, steps):
    count = lax.axis_size(axis)
    first, last = (max(0, -steps), min(count, count - steps))
    return lax.ppermute(value, axis, [(source, source + steps) for source in range(first, last)])


def all_max(value, axes):
    for axis in axes:
        count = lax.axis_size(axis)
        if count & (count - 1):
            value = lax.pmax(value, axis)
            continue
        stride = 1
        while stride < count:
            partner = lax.ppermute(value, axis, [(i, i ^ stride) for i in range(count)])
            value = jnp.maximum(value, partner)
            stride *= 2
    return value


def extended(cells, sides, width):
    for axis, dim in sides:
        count = lax.axis_size(axis)
        ends = count - 1
        head = lax.slice_in_dim(cells, 0, width, axis=dim)
        tail = lax.slice_in_dim(cells, cells.shape[dim] - width, cells.shape[dim], axis=dim)
        cells = jnp.concatenate(
            [
                lax.ppermute(tail, axis, [(i, (i + 1) % count) for i in range(ends)]),
                cells,
                lax.ppermute(head, axis, [((i + 1) % count, i) for i in range(ends)]),
            ],
            axis=dim,
        )
    return cells


def spread_pairs(widened, step_length):
    blocks = {0: widened}
    for row_shift in range(-HALF_EXTENT, HALF_EXTENT + 1):
        if row_shift != 0:
            blocks[row_shift] = passed_along(widened, "row", -row_shift * step_length)
    return jnp.stack([blocks[row_shift] for row_shift in range(-HALF_EXTENT, HALF_EXTENT + 1)])


def return_rows(spill, step_length):
    limit = lax.axis_size("row")
    gathered = spill[HALF_EXTENT]
    for row_shift in range(-HALF_EXTENT, HALF_EXTENT + 1):
        if row_shift != 0 and abs(row_shift) * step_length < limit:
            gathered = gathered + passed_along(
                spill[row_shift + HALF_EXTENT].astype(jnp.bfloat16), "row", row_shift * step_length
            ).astype(jnp.float32)
    return gathered


def head_sums(product, indicator):
    return jnp.einsum("itf,fh->iht", product, indicator, precision=lax.Precision.HIGHEST)


def to_features(per_head):
    return jnp.repeat(jnp.swapaxes(per_head, -1, -2), HD, axis=-1)


LANES = 128


def neighbourhood_body(q_ref, c_ref, kv_ref, mask_ref, att_ref, qg_ref, spill_ref, peak_ref, s_scr):
    f32, bf16 = jnp.float32, jnp.bfloat16
    token_count, feature_count = q_ref.shape
    window = 2 * HALF_EXTENT + 1
    logit_scale = HD ** (-0.5)
    ind = (
        lax.broadcasted_iota(jnp.int32, (feature_count, LANES), 0) // HD
        == lax.broadcasted_iota(jnp.int32, (feature_count, LANES), 1)
    ).astype(bf16)
    ind_t = (
        lax.broadcasted_iota(jnp.int32, (LANES, feature_count), 1) // HD
        == lax.broadcasted_iota(jnp.int32, (LANES, feature_count), 0)
    ).astype(bf16)

    def mm(x, y):
        return jnp.dot(x, y, preferred_element_type=f32)

    def exact_sum(p):
        hi = p.astype(bf16)
        lo = (p - hi.astype(f32)).astype(bf16)
        return mm(hi, ind) + mm(lo, ind)

    def full_sum(p):
        hi = p.astype(bf16)
        r1 = p - hi.astype(f32)
        mid = r1.astype(bf16)
        lo = (r1 - mid.astype(f32)).astype(bf16)
        return mm(hi, ind) + mm(mid, ind) + mm(lo, ind)

    def spread(w):
        return mm(w, ind_t)

    def keys(a, b):
        return kv_ref[a, pl.ds(b * DILATION_STEP, token_count), pl.ds(0, feature_count)].astype(f32)

    def values(a, b):
        return kv_ref[a, pl.ds(b * DILATION_STEP, token_count), pl.ds(feature_count, feature_count)].astype(f32)

    q = q_ref[...].astype(f32)
    c = c_ref[...].astype(f32)
    top = jnp.full((token_count, LANES), big_negative, f32)
    for a in range(window):
        for b in range(window):
            s = exact_sum(q * keys(a, b)) * logit_scale
            s = jnp.where(mask_ref[a * window + b] > 0, s, big_negative)
            s_scr[a * window + b] = s
            top = jnp.maximum(top, s)
    peak_ref[...] = jnp.max(top, axis=0, keepdims=True)
    total = jnp.zeros((token_count, LANES), f32)
    for ab in range(window * window):
        e = jnp.where(mask_ref[ab] > 0, jnp.exp(s_scr[ab] - top), 0.0)
        s_scr[ab] = e
        total = total + e
    att = jnp.zeros((token_count, feature_count), f32)
    for a in range(window):
        for b in range(window):
            w_b = (s_scr[a * window + b] / total).astype(bf16)
            att = att + spread(w_b) * values(a, b)
    att_ref[...] = att.astype(att_ref.dtype)
    drive = full_sum(c * att)
    spill_ref[...] = jnp.zeros(spill_ref.shape, f32)
    qg = jnp.zeros((token_count, feature_count), f32)
    for a in range(window):
        for b in range(window):
            w = s_scr[a * window + b] / total
            v = values(a, b)
            through = exact_sum(c * v)
            slope = spread((w * (through - drive)).astype(bf16))
            qg = qg + slope * keys(a, b)
            rows = pl.ds(b * DILATION_STEP, token_count)
            spill_ref[a, rows, pl.ds(0, feature_count)] += slope * q * logit_scale
            spill_ref[a, rows, pl.ds(feature_count, feature_count)] += spread(w.astype(bf16)) * c
    qg_ref[...] = (qg * logit_scale).astype(qg_ref.dtype)


def neighbourhood_kernel(q, c, kv, mask, interpret=False):
    token_count, feature_count = q.shape
    window = kv.shape[0]
    vmem = pltpu.MemorySpace.VMEM if hasattr(pltpu, "MemorySpace") else pltpu.TPUMemorySpace.VMEM
    spec = pl.BlockSpec(memory_space=vmem)
    return pl.pallas_call(
        neighbourhood_body,
        out_shape=(
            jax.ShapeDtypeStruct((token_count, feature_count), jnp.bfloat16),
            jax.ShapeDtypeStruct((token_count, feature_count), jnp.bfloat16),
            jax.ShapeDtypeStruct(kv.shape, jnp.float32),
            jax.ShapeDtypeStruct((1, LANES), jnp.float32),
        ),
        in_specs=[spec] * 4,
        out_specs=(spec,) * 4,
        scratch_shapes=[pltpu.VMEM((window * window, token_count, LANES), jnp.float32)],
        compiler_params=pltpu.CompilerParams(vmem_limit_bytes=56 * 1024 * 1024),
        interpret=interpret,
    )(q, c, kv, mask)


def on_device(queries, key_vectors, value_vectors, cotangent):
    rows_per_shard, cols_dev, feature_count = queries.shape
    token_count = rows_per_shard * cols_dev
    neighbour_cells = HALF_EXTENT * DILATION_STEP
    step_length = DILATION_STEP // rows_per_shard
    window = 2 * HALF_EXTENT + 1
    logit_scale = HD ** (-0.5)
    row_total = rows_per_shard * lax.axis_size("row")
    col_total = cols_dev * lax.axis_size("col")
    row_place = lax.axis_index("row") * rows_per_shard + jnp.arange(rows_per_shard, dtype=jnp.int32)
    col_place = lax.axis_index("col") * cols_dev + jnp.arange(cols_dev, dtype=jnp.int32)
    shift_list = jnp.arange(-HALF_EXTENT, HALF_EXTENT + 1, dtype=jnp.int32) * DILATION_STEP
    row_target = row_place[None, :] + shift_list[:, None]
    col_target = col_place[None, :] + shift_list[:, None]
    row_usable = (row_target >= 0) & (row_target < row_total)
    col_usable = (col_target >= 0) & (col_target < col_total)
    usable = col_usable[:, None, None, :] & row_usable[None, :, :, None]
    pairs_in = jnp.concatenate([key_vectors, value_vectors], axis=-1)
    stacked = extended(spread_pairs(pairs_in, step_length), (("col", 2),), neighbour_cells)

    tokens = lax.broadcasted_iota(jnp.int32, (window * window, token_count, LANES), 2) < H
    usable_ab = jnp.transpose(usable[:, :, 0, :], (1, 0, 2)).reshape(window * window, token_count)
    mask = jnp.where(tokens, usable_ab[..., None], True).astype(jnp.float32)
    attended, query_grad, spill, peak = neighbourhood_kernel(
        queries.reshape(token_count, feature_count),
        cotangent.reshape(token_count, feature_count),
        stacked.reshape(window, cols_dev + 2 * neighbour_cells, 2 * feature_count),
        mask,
    )
    attended = attended.reshape(rows_per_shard, cols_dev, feature_count)
    query_grad = query_grad.reshape(rows_per_shard, cols_dev, feature_count)
    spill = spill.reshape(window, rows_per_shard, cols_dev + 2 * neighbour_cells, 2 * feature_count)
    west_part = spill[:, :, :neighbour_cells]
    east_part = spill[:, :, neighbour_cells + cols_dev :]
    owned = spill[:, :, neighbour_cells : neighbour_cells + cols_dev]
    from_east = passed_along(west_part.astype(jnp.bfloat16), "col", -1).astype(west_part.dtype)
    from_west = passed_along(east_part.astype(jnp.bfloat16), "col", 1).astype(east_part.dtype)
    peak = all_max(peak[0, :H], ("col",))
    peak, from_east, from_west = lax.optimization_barrier((peak, from_east, from_west))
    owned = owned.at[:, :, cols_dev - neighbour_cells :].add(from_east)
    owned = owned.at[:, :, :neighbour_cells].add(from_west)
    owned = return_rows(owned, step_length)
    logit_peak = all_max(peak, ("row",))
    key_grad = owned[..., :feature_count].astype(jnp.bfloat16)
    value_grad = owned[..., feature_count:].astype(jnp.bfloat16)
    return (attended, query_grad, key_grad, value_grad, logit_peak)


def solution(mesh):
    placed = (
        P("row", "col", None),
        P("row", "col", None),
        P("row", "col", None),
        P("row", "col", None),
    )
    return jax.shard_map(
        on_device,
        mesh=mesh,
        in_specs=placed,
        out_specs=(
            P("row", "col", None),
            P("row", "col", None),
            P("row", "col", None),
            P("row", "col", None),
            P(),
        ),
        check_vma=False,
    )
```

```python
import jax
import jax.numpy as jnp
from jax import lax
from jax.sharding import PartitionSpec as P
from jax.experimental import pallas as pl
from jax.experimental.pallas import tpu as pltpu

H = 12
HD = 64
DILATION_STEP = 16
HALF_EXTENT = 3


big_negative = -1e30


def passed_along(value, axis, steps):
    count = lax.axis_size(axis)
    first, last = (max(0, -steps), min(count, count - steps))
    return lax.ppermute(value, axis, [(source, source + steps) for source in range(first, last)])


def all_max(value, axes):
    for axis in axes:
        count = lax.axis_size(axis)
        if count & (count - 1):
            value = lax.pmax(value, axis)
            continue
        stride = 1
        while stride < count:
            partner = lax.ppermute(value, axis, [(i, i ^ stride) for i in range(count)])
            value = jnp.maximum(value, partner)
            stride *= 2
    return value


def extended(cells, sides, width):
    for axis, dim in sides:
        count = lax.axis_size(axis)
        ends = count - 1
        head = lax.slice_in_dim(cells, 0, width, axis=dim)
        tail = lax.slice_in_dim(cells, cells.shape[dim] - width, cells.shape[dim], axis=dim)
        cells = jnp.concatenate(
            [
                lax.ppermute(tail, axis, [(i, (i + 1) % count) for i in range(ends)]),
                cells,
                lax.ppermute(head, axis, [((i + 1) % count, i) for i in range(ends)]),
            ],
            axis=dim,
        )
    return cells


def spread_pairs(widened, step_length):
    blocks = {0: widened}
    for row_shift in range(-HALF_EXTENT, HALF_EXTENT + 1):
        if row_shift != 0:
            blocks[row_shift] = passed_along(widened, "row", -row_shift * step_length)
    return jnp.stack([blocks[row_shift] for row_shift in range(-HALF_EXTENT, HALF_EXTENT + 1)])


def return_rows(spill, step_length):
    limit = lax.axis_size("row")
    gathered = spill[HALF_EXTENT]
    for row_shift in range(-HALF_EXTENT, HALF_EXTENT + 1):
        if row_shift != 0 and abs(row_shift) * step_length < limit:
            gathered = gathered + passed_along(
                spill[row_shift + HALF_EXTENT].astype(jnp.bfloat16), "row", row_shift * step_length
            ).astype(jnp.float32)
    return gathered


def head_sums(product, indicator):
    return jnp.einsum("itf,fh->iht", product, indicator, precision=lax.Precision.HIGHEST)


def to_features(per_head):
    return jnp.repeat(jnp.swapaxes(per_head, -1, -2), HD, axis=-1)


LANES = 128


def neighbourhood_body(q_ref, c_ref, kv_ref, mask_ref, att_ref, qg_ref, spill_ref, peak_ref, s_scr):
    f32, bf16 = jnp.float32, jnp.bfloat16
    token_count, feature_count = q_ref.shape
    window = 2 * HALF_EXTENT + 1
    logit_scale = HD ** (-0.5)
    ind = (
        lax.broadcasted_iota(jnp.int32, (feature_count, LANES), 0) // HD
        == lax.broadcasted_iota(jnp.int32, (feature_count, LANES), 1)
    ).astype(bf16)
    ind_t = (
        lax.broadcasted_iota(jnp.int32, (LANES, feature_count), 1) // HD
        == lax.broadcasted_iota(jnp.int32, (LANES, feature_count), 0)
    ).astype(bf16)

    def mm(x, y):
        return jnp.dot(x, y, preferred_element_type=f32)

    def exact_sum(p):
        hi = p.astype(bf16)
        lo = (p - hi.astype(f32)).astype(bf16)
        return mm(hi, ind) + mm(lo, ind)

    def full_sum(p):
        hi = p.astype(bf16)
        r1 = p - hi.astype(f32)
        mid = r1.astype(bf16)
        lo = (r1 - mid.astype(f32)).astype(bf16)
        return mm(hi, ind) + mm(mid, ind) + mm(lo, ind)

    def spread(w):
        return mm(w, ind_t)

    def keys(a, b):
        return kv_ref[a, pl.ds(b * DILATION_STEP, token_count), pl.ds(0, feature_count)].astype(f32)

    def values(a, b):
        return kv_ref[a, pl.ds(b * DILATION_STEP, token_count), pl.ds(feature_count, feature_count)].astype(f32)

    q = q_ref[...].astype(f32)
    c = c_ref[...].astype(f32)
    def score_row(a, top):
        for b in range(window):
            s = exact_sum(q * keys(a, b)) * logit_scale
            s = jnp.where(mask_ref[a * window + b] > 0, s, big_negative)
            s_scr[a * window + b] = s
            top = jnp.maximum(top, s)
        return top

    top = lax.fori_loop(0, window, score_row, jnp.full((token_count, LANES), big_negative, f32))
    peak_ref[...] = jnp.max(top, axis=0, keepdims=True)
    total = jnp.zeros((token_count, LANES), f32)
    for ab in range(window * window):
        e = jnp.where(mask_ref[ab] > 0, jnp.exp(s_scr[ab] - top), 0.0)
        s_scr[ab] = e
        total = total + e
    def attend_row(a, att):
        for b in range(window):
            w_b = (s_scr[a * window + b] / total).astype(bf16)
            att = att + spread(w_b) * values(a, b)
        return att

    att = lax.fori_loop(0, window, attend_row, jnp.zeros((token_count, feature_count), f32))
    att_ref[...] = att.astype(att_ref.dtype)
    drive = full_sum(c * att)
    spill_ref[...] = jnp.zeros(spill_ref.shape, f32)
    def slope_row(a, qg):
        for b in range(window):
            w = s_scr[a * window + b] / total
            v = values(a, b)
            through = exact_sum(c * v)
            slope = spread((w * (through - drive)).astype(bf16))
            qg = qg + slope * keys(a, b)
            rows = pl.ds(b * DILATION_STEP, token_count)
            spill_ref[a, rows, pl.ds(0, feature_count)] += slope * q * logit_scale
            spill_ref[a, rows, pl.ds(feature_count, feature_count)] += spread(w.astype(bf16)) * c
        return qg

    qg = lax.fori_loop(0, window, slope_row, jnp.zeros((token_count, feature_count), f32))
    qg_ref[...] = (qg * logit_scale).astype(qg_ref.dtype)


def neighbourhood_kernel(q, c, kv, mask, interpret=False):
    token_count, feature_count = q.shape
    window = kv.shape[0]
    vmem = pltpu.MemorySpace.VMEM if hasattr(pltpu, "MemorySpace") else pltpu.TPUMemorySpace.VMEM
    spec = pl.BlockSpec(memory_space=vmem)
    return pl.pallas_call(
        neighbourhood_body,
        out_shape=(
            jax.ShapeDtypeStruct((token_count, feature_count), jnp.bfloat16),
            jax.ShapeDtypeStruct((token_count, feature_count), jnp.bfloat16),
            jax.ShapeDtypeStruct(kv.shape, jnp.float32),
            jax.ShapeDtypeStruct((1, LANES), jnp.float32),
        ),
        in_specs=[spec] * 4,
        out_specs=(spec,) * 4,
        scratch_shapes=[pltpu.VMEM((window * window, token_count, LANES), jnp.float32)],
        compiler_params=pltpu.CompilerParams(vmem_limit_bytes=56 * 1024 * 1024),
        interpret=interpret,
    )(q, c, kv, mask)


def on_device(queries, key_vectors, value_vectors, cotangent):
    rows_per_shard, cols_dev, feature_count = queries.shape
    token_count = rows_per_shard * cols_dev
    neighbour_cells = HALF_EXTENT * DILATION_STEP
    step_length = DILATION_STEP // rows_per_shard
    window = 2 * HALF_EXTENT + 1
    logit_scale = HD ** (-0.5)
    row_total = rows_per_shard * lax.axis_size("row")
    col_total = cols_dev * lax.axis_size("col")
    row_place = lax.axis_index("row") * rows_per_shard + jnp.arange(rows_per_shard, dtype=jnp.int32)
    col_place = lax.axis_index("col") * cols_dev + jnp.arange(cols_dev, dtype=jnp.int32)
    shift_list = jnp.arange(-HALF_EXTENT, HALF_EXTENT + 1, dtype=jnp.int32) * DILATION_STEP
    row_target = row_place[None, :] + shift_list[:, None]
    col_target = col_place[None, :] + shift_list[:, None]
    row_usable = (row_target >= 0) & (row_target < row_total)
    col_usable = (col_target >= 0) & (col_target < col_total)
    usable = col_usable[:, None, None, :] & row_usable[None, :, :, None]
    pairs_in = jnp.concatenate([key_vectors, value_vectors], axis=-1)
    stacked = extended(spread_pairs(pairs_in, step_length), (("col", 2),), neighbour_cells)

    tokens = lax.broadcasted_iota(jnp.int32, (window * window, token_count, LANES), 2) < H
    usable_ab = jnp.transpose(usable[:, :, 0, :], (1, 0, 2)).reshape(window * window, token_count)
    mask = jnp.where(tokens, usable_ab[..., None], True).astype(jnp.float32)
    attended, query_grad, spill, peak = neighbourhood_kernel(
        queries.reshape(token_count, feature_count),
        cotangent.reshape(token_count, feature_count),
        stacked.reshape(window, cols_dev + 2 * neighbour_cells, 2 * feature_count),
        mask,
    )
    attended = attended.reshape(rows_per_shard, cols_dev, feature_count)
    query_grad = query_grad.reshape(rows_per_shard, cols_dev, feature_count)
    spill = spill.reshape(window, rows_per_shard, cols_dev + 2 * neighbour_cells, 2 * feature_count)
    west_part = spill[:, :, :neighbour_cells]
    east_part = spill[:, :, neighbour_cells + cols_dev :]
    owned = spill[:, :, neighbour_cells : neighbour_cells + cols_dev]
    from_east = passed_along(west_part.astype(jnp.bfloat16), "col", -1).astype(west_part.dtype)
    from_west = passed_along(east_part.astype(jnp.bfloat16), "col", 1).astype(east_part.dtype)
    peak = all_max(peak[0, :H], ("col",))
    peak, from_east, from_west = lax.optimization_barrier((peak, from_east, from_west))
    owned = owned.at[:, :, cols_dev - neighbour_cells :].add(from_east)
    owned = owned.at[:, :, :neighbour_cells].add(from_west)
    owned = return_rows(owned, step_length)
    logit_peak = all_max(peak, ("row",))
    key_grad = owned[..., :feature_count].astype(jnp.bfloat16)
    value_grad = owned[..., feature_count:].astype(jnp.bfloat16)
    return (attended, query_grad, key_grad, value_grad, logit_peak)


def solution(mesh):
    placed = (
        P("row", "col", None),
        P("row", "col", None),
        P("row", "col", None),
        P("row", "col", None),
    )
    return jax.shard_map(
        on_device,
        mesh=mesh,
        in_specs=placed,
        out_specs=(
            P("row", "col", None),
            P("row", "col", None),
            P("row", "col", None),
            P("row", "col", None),
            P(),
        ),
        check_vma=False,
    )
```
